512 devices in a mesh: gz: 16 (over z), gx: 8 (over y, core), gy: 4 (over x).
Axes of the slice: x: 4, y: 4, z: 16, core: 2. Of those that a mesh axis runs over, the one named last changes fastest.
Arguments:
- hydro_state: float32 [8, 128, 128, 2048], P(None, 'gx', 'gy', 'gz'), may hold values from -0.5 to 2, as said below
- material_id: int32 [128, 128, 2048], P('gx', 'gy', 'gz'), may hold values from 0 to 3
- block_mask: int32 [4, 4, 64], replicated, may hold values 0 or 1
Outputs:
- hydro_next: float32 [8, 128, 128, 2048], P(None, 'gx', 'gy', 'gz')
The draws below stay inside these ranges and needn't reach their ends.
Inputs may be any that keep to these rules, and one draw needn't show every extreme that they name: `hydro_state`: field 0 lies in 0.9 to 2.0, fields 1 to 3 in -0.5 to 0.5, field 4 in 0.25 to 1.5, fields 5 and 7 in 0 to 1, field 6 in 0 to 0.5.
All inputs are finite; a program needn't handle non-finite values. Where the reference program divides by a largest or mean magnitude, that divisor is 1e-20 or more.
Results may differ from the reference program's by a relative error of at most 0.00011.
Values sent between devices are 32-bit elements; how exact they have to be, the bound alone decides.
No kernel may reach another device: no remote copies, remote signals or barrier semaphores. Data moves between devices by JAX's collectives and lax.ppermute only.
A program may use at most 128 MiB of HBM per device.

```python
import jax
import jax.numpy as jnp

B = 32
CYCLES = 2
NMAT = 4
NX = 128
NY = 128
NZ = 2048


def draw_hydro_state(key, part):
    subkeys = jax.random.split(key, 9)
    grid_shape = (NX, NY, NZ)
    centre = jax.random.uniform(subkeys[6], (), jnp.float32, 0.2, 0.8)
    speed_peak = jax.random.uniform(subkeys[7], (), jnp.float32, 0.6, 1.0)
    density_peak = jax.random.uniform(subkeys[8], (), jnp.float32, 0.5, 1.0)
    position = (jnp.arange(NZ, dtype=jnp.float32) + 0.5) / NZ
    profile = jnp.exp(-jnp.square((position - centre) / 0.12))
    speed_factor = (0.2 + 0.8 * speed_peak * profile)[None, None, None, :]
    density_span = (0.2 + 0.9 * density_peak * profile)[None, None, :]
    density = 0.9 + density_span * jax.random.uniform(subkeys[0], grid_shape, jnp.float32, 0.0, 1.0)
    velocity = jnp.clip(0.25 * jax.random.normal(subkeys[1], (3,) + grid_shape, jnp.float32), -0.5, 0.5) * speed_factor
    energy = jax.random.uniform(subkeys[2], grid_shape, jnp.float32, 0.5, 1.5)
    fraction = jax.random.uniform(subkeys[3], grid_shape, jnp.float32, 0.0, 1.0)
    plastic = jax.random.uniform(subkeys[4], grid_shape, jnp.float32, 0.0, 0.5)
    damage = jax.random.uniform(subkeys[5], grid_shape, jnp.float32, 0.0, 1.0)
    return jnp.concatenate([density[None], velocity, energy[None], fraction[None], plastic[None], damage[None]])


def touch_ends(entries, rng, least, high):
    spot = [jax.random.randint(jax.random.fold_in(rng, axis), (), 0, length) for axis, length in enumerate(entries.shape)]
    main_axis = entries.shape.index(max(entries.shape))
    beside = spot[:main_axis] + [(spot[main_axis] + 1) % entries.shape[main_axis]] + spot[main_axis + 1:]
    return entries.at[tuple(spot)].set(least).at[tuple(beside)].set(high)


def setup_inputs(seed: int = 0) -> dict:
    keys = jax.random.split(jax.random.key(seed), 4)
    return {
        "hydro_state": draw_hydro_state(jax.random.fold_in(keys[3], 71), 0),
        "material_id": touch_ends(jax.random.randint(keys[1], (NX, NY, NZ), 0, NMAT), jax.random.fold_in(keys[1], 1), 0, NMAT - 1).astype(jnp.int32),
        "block_mask": touch_ends((jax.random.randint(keys[2], (NX // B, NY // B, NZ // B), 0, 5) < 3).astype(jnp.int32), jax.random.fold_in(keys[2], 1), 0, 1),
    }


courant = 0.15
visc_quad = 2.0
visc_linear = 0.5
rest_density = (1.0, 1.25, 1.5, 1.8)
sound_base = (1.0, 0.8, 1.2, 0.9)
hugoniot_slope = (1.5, 1.4, 1.2, 1.6)
gruneisen = (2.0, 1.7, 1.6, 2.2)


def lookup(material, values):
    result = jnp.zeros(material.shape, jnp.float32)
    for number, amount in enumerate(values):
        result = result + jnp.where(material == number, jnp.float32(amount), jnp.float32(0.0))
    return result


def equation_of_state(density, energy, material):
    rest_rho = lookup(material, rest_density)
    sound_zero = lookup(material, sound_base)
    slope_mat = lookup(material, hugoniot_slope)
    gamma_mat = lookup(material, gruneisen)
    strain = 1.0 - rest_rho / density
    squeeze = jnp.maximum(strain, 0.0)
    hugoniot = rest_rho * sound_zero * sound_zero * strain * (1.0 + 2.0 * slope_mat * squeeze + 3.0 * slope_mat * slope_mat * squeeze * squeeze)
    pressure = hugoniot * (1.0 - 0.5 * gamma_mat * strain) + gamma_mat * density * energy
    sound_speed = sound_zero * (1.0 + slope_mat * squeeze)
    return pressure, sound_speed


def shifted(padded, spatial_axis, offset):
    starts = [1, 1, 1]
    starts[spatial_axis] = 1 + offset
    return padded[..., starts[0]:starts[0] + padded.shape[-3] - 2, starts[1]:starts[1] + padded.shape[-2] - 2, starts[2]:starts[2] + padded.shape[-1] - 2]


def stress_terms(velocity_pad, density, pressure, sound_speed):
    gradient = [(shifted(velocity_pad, column, 1) - shifted(velocity_pad, column, -1)) * 0.5 for column in range(3)]
    diverge = gradient[0][0] + gradient[1][1] + gradient[2][2]
    strain_xy = 0.5 * (gradient[1][0] + gradient[0][1])
    strain_xz = 0.5 * (gradient[2][0] + gradient[0][2])
    strain_yz = 0.5 * (gradient[2][1] + gradient[1][2])
    squares = gradient[0][0] * gradient[0][0] + gradient[1][1] * gradient[1][1] + gradient[2][2] * gradient[2][2]
    squares = squares + 2.0 * (strain_xy * strain_xy + strain_xz * strain_xz + strain_yz * strain_yz)
    compress = jnp.maximum(-diverge, 0.0)
    viscosity = density * compress * (visc_quad * compress + visc_linear * sound_speed)
    stress = jnp.stack([-pressure + viscosity * gradient[0][0], -pressure + viscosity * gradient[1][1], -pressure + viscosity * gradient[2][2], viscosity * strain_xy, viscosity * strain_xz, viscosity * strain_yz])
    power = -pressure * diverge + viscosity * squares
    heating = viscosity * squares
    return stress, diverge, power, heating


def acceleration(stress_pad, density):
    component_rows = ((0, 3, 4), (3, 1, 5), (4, 5, 2))
    results = []
    for comps in component_rows:
        total = jnp.zeros(density.shape, jnp.float32)
        for column in range(3):
            total = total + shifted(stress_pad[comps[column]], column, 1) - shifted(stress_pad[comps[column]], column, -1)
        results.append(0.5 * total / density)
    return jnp.stack(results)


def lagrange(state_part, density, accel, diverge, power, heating, step_dt):
    new_density = density / (1.0 + step_dt * diverge)
    velocity = state_part[1:4] + step_dt * accel
    energy = state_part[4] + step_dt * power / density
    plastic = state_part[6] + step_dt * heating / density
    return jnp.concatenate([new_density[None], new_density[None] * velocity, (new_density * energy)[None], (new_density * state_part[5])[None], (new_density * plastic)[None], (new_density * state_part[7])[None]])


def remap(conserved_pad, velocity_pad, step_dt):
    centre = shifted(conserved_pad, 0, 0)
    total = centre
    for column in range(3):
        middle_vel = shifted(velocity_pad[column], column, 0)
        ahead_vel = shifted(velocity_pad[column], column, 1)
        behind_vel = shifted(velocity_pad[column], column, -1)
        upper = step_dt * 0.5 * (middle_vel + ahead_vel)
        lower = step_dt * 0.5 * (behind_vel + middle_vel)
        flux_up = jnp.maximum(upper, 0.0) * centre + jnp.minimum(upper, 0.0) * shifted(conserved_pad, column, 1)
        flux_down = jnp.maximum(lower, 0.0) * shifted(conserved_pad, column, -1) + jnp.minimum(lower, 0.0) * centre
        total = total - (flux_up - flux_down)
    density = total[0]
    return jnp.concatenate([density[None], total[1:] / density])


def cell_mask(block_mask, edge):
    count_x, count_y, count_z = block_mask.shape
    spread = jnp.broadcast_to(block_mask[:, None, :, None, :, None], (count_x, edge, count_y, edge, count_z, edge))
    return spread.reshape(count_x * edge, count_y * edge, count_z * edge) > 0


def pad_one(array_in):
    return jnp.pad(array_in, ((0, 0), (1, 1), (1, 1), (1, 1)))


def reference(hydro_state, material_id, block_mask):
    active = cell_mask(block_mask, B)
    state_now = hydro_state
    for cycle_number in range(CYCLES):
        pressure, sound_speed = equation_of_state(state_now[0], state_now[4], material_id)
        fastest = jnp.max(sound_speed + jnp.abs(state_now[1]) + jnp.abs(state_now[2]) + jnp.abs(state_now[3]))
        step_dt = courant / fastest
        velocity_pad = pad_one(state_now[1:4])
        stress, diverge, power, heating = stress_terms(velocity_pad, state_now[0], pressure, sound_speed)
        accel = acceleration(pad_one(stress), state_now[0])
        conserved = lagrange(state_now, state_now[0], accel, diverge, power, heating, step_dt)
        remapped = remap(pad_one(conserved), velocity_pad, step_dt)
        state_now = jnp.where(active[None], remapped, state_now)
    return state_now
```

```python
import jax
import jax.numpy as jnp
from jax import lax
from jax.sharding import PartitionSpec as P

B = 32
CYCLES = 2


courant = 0.15
visc_quad = 2.0
visc_linear = 0.5
rest_density = (1.0, 1.25, 1.5, 1.8)
sound_base = (1.0, 0.8, 1.2, 0.9)
hugoniot_slope = (1.5, 1.4, 1.2, 1.6)
gruneisen = (2.0, 1.7, 1.6, 2.2)

SPATIAL = (("gx", 1), ("gy", 2), ("gz", 3))
STRESS_ROWS = ((0, 3, 4), (3, 1, 5), (4, 5, 2))


def faces(array, j):
    axis, dim = SPATIAL[j]
    peers, length = lax.axis_size(axis), array.shape[dim]
    up = [(i, i + 1) for i in range(peers - 1)]
    down = [(i + 1, i) for i in range(peers - 1)]
    first = lax.slice_in_dim(array, 0, 1, axis=dim)
    last = lax.slice_in_dim(array, length - 1, length, axis=dim)
    from_prev = lax.ppermute(last, axis, up)
    from_next = lax.ppermute(first, axis, down)
    return from_next, from_prev


def plus(array, j, from_next):
    dim = SPATIAL[j][1] - (4 - array.ndim)
    length = array.shape[dim]
    return jnp.concatenate([lax.slice_in_dim(array, 1, length, axis=dim), from_next], axis=dim)


def minus(array, j, from_prev):
    dim = SPATIAL[j][1] - (4 - array.ndim)
    length = array.shape[dim]
    return jnp.concatenate([from_prev, lax.slice_in_dim(array, 0, length - 1, axis=dim)], axis=dim)


def lookup(material, values):
    result = jnp.zeros(material.shape, jnp.float32)
    for number, amount in enumerate(values):
        result = result + jnp.where(material == number, jnp.float32(amount), jnp.float32(0.0))
    return result


def equation_of_state(density, energy, material):
    rest_rho = lookup(material, rest_density)
    sound_zero = lookup(material, sound_base)
    slope_mat = lookup(material, hugoniot_slope)
    gamma_mat = lookup(material, gruneisen)
    strain = 1.0 - rest_rho / density
    squeeze = jnp.maximum(strain, 0.0)
    hugoniot = (
        rest_rho
        * sound_zero
        * sound_zero
        * strain
        * (1.0 + 2.0 * slope_mat * squeeze + 3.0 * slope_mat * slope_mat * squeeze * squeeze)
    )
    pressure = hugoniot * (1.0 - 0.5 * gamma_mat * strain) + gamma_mat * density * energy
    sound_speed = sound_zero * (1.0 + slope_mat * squeeze)
    return (pressure, sound_speed)


def stress_terms(velocity, vel_faces, density, pressure, sound_speed):
    gradient = [
        (plus(velocity, column, vel_faces[column][0]) - minus(velocity, column, vel_faces[column][1])) * 0.5
        for column in range(3)
    ]
    diverge = gradient[0][0] + gradient[1][1] + gradient[2][2]
    strain_xy = 0.5 * (gradient[1][0] + gradient[0][1])
    strain_xz = 0.5 * (gradient[2][0] + gradient[0][2])
    strain_yz = 0.5 * (gradient[2][1] + gradient[1][2])
    squares = (
        gradient[0][0] * gradient[0][0]
        + gradient[1][1] * gradient[1][1]
        + gradient[2][2] * gradient[2][2]
    )
    squares = squares + 2.0 * (
        strain_xy * strain_xy + strain_xz * strain_xz + strain_yz * strain_yz
    )
    compress = jnp.maximum(-diverge, 0.0)
    viscosity = density * compress * (visc_quad * compress + visc_linear * sound_speed)
    stress = [
        -pressure + viscosity * gradient[0][0],
        -pressure + viscosity * gradient[1][1],
        -pressure + viscosity * gradient[2][2],
        viscosity * strain_xy,
        viscosity * strain_xz,
        viscosity * strain_yz,
    ]
    power = -pressure * diverge + viscosity * squares
    heating = viscosity * squares
    return (stress, diverge, power, heating)


def acceleration(stress, density):
    stress_faces = []
    for column in range(3):
        picked = jnp.stack([stress[c] for c in STRESS_ROWS[column]])
        stress_faces.append((picked, faces(picked, column)))
    results = []
    for row in range(3):
        total = jnp.zeros(density.shape, jnp.float32)
        for column in range(3):
            picked, (from_next, from_prev) = stress_faces[column]
            slot = STRESS_ROWS[column].index(STRESS_ROWS[row][column])
            comp = stress[STRESS_ROWS[row][column]]
            total = total + plus(comp, column, from_next[slot]) - minus(comp, column, from_prev[slot])
        results.append(0.5 * total / density)
    return jnp.stack(results)


def lagrange(state_part, density, accel, diverge, power, heating, step_dt):
    new_density = density / (1.0 + step_dt * diverge)
    velocity = state_part[1:4] + step_dt * accel
    energy = state_part[4] + step_dt * power / density
    plastic = state_part[6] + step_dt * heating / density
    return jnp.concatenate(
        [
            new_density[None],
            new_density[None] * velocity,
            (new_density * energy)[None],
            (new_density * state_part[5])[None],
            (new_density * plastic)[None],
            (new_density * state_part[7])[None],
        ]
    )


def remap(conserved, velocity, vel_faces, step_dt):
    centre = conserved
    total = centre
    for column in range(3):
        cons_next, cons_prev = faces(conserved, column)
        middle_vel = velocity[column]
        ahead_vel = plus(velocity[column], column, vel_faces[column][0][column])
        behind_vel = minus(velocity[column], column, vel_faces[column][1][column])
        upper = step_dt * 0.5 * (middle_vel + ahead_vel)
        lower = step_dt * 0.5 * (behind_vel + middle_vel)
        flux_up = jnp.maximum(upper, 0.0) * centre + jnp.minimum(upper, 0.0) * plus(
            conserved, column, cons_next
        )
        flux_down = (
            jnp.maximum(lower, 0.0) * minus(conserved, column, cons_prev)
            + jnp.minimum(lower, 0.0) * centre
        )
        total = total - (flux_up - flux_down)
    density = total[0]
    return jnp.concatenate([density[None], total[1:] / density])


def block_picks(position, extent, count):
    cells = position * extent + jnp.arange(extent, dtype=jnp.int32)
    return (cells[:, None] // B == jnp.arange(count, dtype=jnp.int32)[None, :]).astype(jnp.float32)


def local_active(block_mask, extent_x, extent_y, extent_z):
    count_x, count_y, count_z = block_mask.shape
    pick_x = block_picks(lax.axis_index("gx"), extent_x, count_x)
    pick_y = block_picks(lax.axis_index("gy"), extent_y, count_y)
    pick_z = block_picks(lax.axis_index("gz"), extent_z, count_z)
    present = (block_mask > 0).astype(jnp.float32)
    along_z = jnp.dot(
        present.reshape(count_x * count_y, count_z), pick_z.T, precision=lax.Precision.HIGHEST
    ).reshape(count_x, count_y, extent_z)
    along_y = jnp.einsum("jb,abk->ajk", pick_y, along_z, precision=lax.Precision.HIGHEST)
    spread = jnp.einsum("ia,ajk->ijk", pick_x, along_y, precision=lax.Precision.HIGHEST)
    return spread > 0.5


def global_max(value):
    for axis in ("gy", "gx", "gz"):
        value = lax.pmax(value, axis)
    return value


def local(hydro_state, material_id, block_mask):
    extent_x, extent_y, extent_z = material_id.shape
    active = local_active(block_mask, extent_x, extent_y, extent_z)
    state_now = hydro_state
    for cycle_number in range(CYCLES):
        pressure, sound_speed = equation_of_state(state_now[0], state_now[4], material_id)
        velocity = state_now[1:4]
        vel_faces = [faces(velocity, column) for column in range(3)]
        local_fast = jnp.max(
            sound_speed + jnp.abs(state_now[1]) + jnp.abs(state_now[2]) + jnp.abs(state_now[3])
        )
        fastest = global_max(local_fast)
        step_dt = courant / fastest
        stress, diverge, power, heating = stress_terms(
            velocity, vel_faces, state_now[0], pressure, sound_speed
        )
        accel = acceleration(stress, state_now[0])
        conserved = lagrange(state_now, state_now[0], accel, diverge, power, heating, step_dt)
        remapped = remap(conserved, velocity, vel_faces, step_dt)
        state_now = jnp.where(active[None], remapped, state_now)
    return state_now


def solution(mesh):
    in_specs = (P(None, "gx", "gy", "gz"), P("gx", "gy", "gz"), P())
    out_specs = P(None, "gx", "gy", "gz")
    return jax.shard_map(local, mesh=mesh, in_specs=in_specs, out_specs=out_specs, check_vma=False)
```

```python
import jax
import jax.numpy as jnp
from jax import lax
from jax.sharding import PartitionSpec as P

B = 32
CYCLES = 2


courant = 0.15
visc_quad = 2.0
visc_linear = 0.5
rest_density = (1.0, 1.25, 1.5, 1.8)
sound_base = (1.0, 0.8, 1.2, 0.9)
hugoniot_slope = (1.5, 1.4, 1.2, 1.6)
gruneisen = (2.0, 1.7, 1.6, 2.2)

SPATIAL = (("gx", 1), ("gy", 2), ("gz", 3))
STRESS_ROWS = ((0, 3, 4), (3, 1, 5), (4, 5, 2))


def faces(array, j):
    axis, dim = SPATIAL[j]
    peers, length = lax.axis_size(axis), array.shape[dim]
    up = [(i, i + 1) for i in range(peers - 1)]
    down = [(i + 1, i) for i in range(peers - 1)]
    first = lax.slice_in_dim(array, 0, 1, axis=dim)
    last = lax.slice_in_dim(array, length - 1, length, axis=dim)
    from_prev = lax.ppermute(last, axis, up)
    from_next = lax.ppermute(first, axis, down)
    return from_next, from_prev


def plus(array, j, from_next):
    dim = SPATIAL[j][1] - (4 - array.ndim)
    length = array.shape[dim]
    return jnp.concatenate([lax.slice_in_dim(array, 1, length, axis=dim), from_next], axis=dim)


def minus(array, j, from_prev):
    dim = SPATIAL[j][1] - (4 - array.ndim)
    length = array.shape[dim]
    return jnp.concatenate([from_prev, lax.slice_in_dim(array, 0, length - 1, axis=dim)], axis=dim)


def lookup(material, values):
    result = jnp.zeros(material.shape, jnp.float32)
    for number, amount in enumerate(values):
        result = result + jnp.where(material == number, jnp.float32(amount), jnp.float32(0.0))
    return result


def equation_of_state(density, energy, material):
    rest_rho = lookup(material, rest_density)
    sound_zero = lookup(material, sound_base)
    slope_mat = lookup(material, hugoniot_slope)
    gamma_mat = lookup(material, gruneisen)
    strain = 1.0 - rest_rho / density
    squeeze = jnp.maximum(strain, 0.0)
    hugoniot = (
        rest_rho
        * sound_zero
        * sound_zero
        * strain
        * (1.0 + 2.0 * slope_mat * squeeze + 3.0 * slope_mat * slope_mat * squeeze * squeeze)
    )
    pressure = hugoniot * (1.0 - 0.5 * gamma_mat * strain) + gamma_mat * density * energy
    sound_speed = sound_zero * (1.0 + slope_mat * squeeze)
    return (pressure, sound_speed)


def stress_terms(velocity, vel_faces, density, pressure, sound_speed):
    gradient = [
        (plus(velocity, column, vel_faces[column][0]) - minus(velocity, column, vel_faces[column][1])) * 0.5
        for column in range(3)
    ]
    diverge = gradient[0][0] + gradient[1][1] + gradient[2][2]
    strain_xy = 0.5 * (gradient[1][0] + gradient[0][1])
    strain_xz = 0.5 * (gradient[2][0] + gradient[0][2])
    strain_yz = 0.5 * (gradient[2][1] + gradient[1][2])
    squares = (
        gradient[0][0] * gradient[0][0]
        + gradient[1][1] * gradient[1][1]
        + gradient[2][2] * gradient[2][2]
    )
    squares = squares + 2.0 * (
        strain_xy * strain_xy + strain_xz * strain_xz + strain_yz * strain_yz
    )
    compress = jnp.maximum(-diverge, 0.0)
    viscosity = density * compress * (visc_quad * compress + visc_linear * sound_speed)
    stress = [
        -pressure + viscosity * gradient[0][0],
        -pressure + viscosity * gradient[1][1],
        -pressure + viscosity * gradient[2][2],
        viscosity * strain_xy,
        viscosity * strain_xz,
        viscosity * strain_yz,
    ]
    power = -pressure * diverge + viscosity * squares
    heating = viscosity * squares
    return (stress, diverge, power, heating)


def acceleration(stress, density):
    stress_faces = []
    for column in range(3):
        picked = jnp.stack([stress[c] for c in STRESS_ROWS[column]])
        stress_faces.append((picked, faces(picked, column)))
    results = []
    for row in range(3):
        total = jnp.zeros(density.shape, jnp.float32)
        for column in range(3):
            picked, (from_next, from_prev) = stress_faces[column]
            slot = STRESS_ROWS[column].index(STRESS_ROWS[row][column])
            comp = stress[STRESS_ROWS[row][column]]
            total = total + plus(comp, column, from_next[slot]) - minus(comp, column, from_prev[slot])
        results.append(0.5 * total / density)
    return jnp.stack(results)


def lagrange(state_part, density, accel, diverge, power, heating, step_dt):
    new_density = density / (1.0 + step_dt * diverge)
    velocity = state_part[1:4] + step_dt * accel
    energy = state_part[4] + step_dt * power / density
    plastic = state_part[6] + step_dt * heating / density
    return jnp.concatenate(
        [
            new_density[None],
            new_density[None] * velocity,
            (new_density * energy)[None],
            (new_density * state_part[5])[None],
            (new_density * plastic)[None],
            (new_density * state_part[7])[None],
        ]
    )


def remap(conserved, velocity, vel_faces, step_dt):
    centre = conserved
    total = centre
    for column in range(3):
        cons_next, cons_prev = faces(conserved, column)
        middle_vel = velocity[column]
        ahead_vel = plus(velocity[column], column, vel_faces[column][0][column])
        behind_vel = minus(velocity[column], column, vel_faces[column][1][column])
        upper = step_dt * 0.5 * (middle_vel + ahead_vel)
        lower = step_dt * 0.5 * (behind_vel + middle_vel)
        flux_up = jnp.maximum(upper, 0.0) * centre + jnp.minimum(upper, 0.0) * plus(
            conserved, column, cons_next
        )
        flux_down = (
            jnp.maximum(lower, 0.0) * minus(conserved, column, cons_prev)
            + jnp.minimum(lower, 0.0) * centre
        )
        total = total - (flux_up - flux_down)
    density = total[0]
    return jnp.concatenate([density[None], total[1:] / density])


def block_picks(position, extent, count):
    cells = position * extent + jnp.arange(extent, dtype=jnp.int32)
    return (cells[:, None] // B == jnp.arange(count, dtype=jnp.int32)[None, :]).astype(jnp.float32)


def local_active(block_mask, extent_x, extent_y, extent_z):
    count_x, count_y, count_z = block_mask.shape
    pick_x = block_picks(lax.axis_index("gx"), extent_x, count_x)
    pick_y = block_picks(lax.axis_index("gy"), extent_y, count_y)
    pick_z = block_picks(lax.axis_index("gz"), extent_z, count_z)
    present = (block_mask > 0).astype(jnp.float32)
    along_z = jnp.dot(
        present.reshape(count_x * count_y, count_z), pick_z.T, precision=lax.Precision.HIGHEST
    ).reshape(count_x, count_y, extent_z)
    along_y = jnp.einsum("jb,abk->ajk", pick_y, along_z, precision=lax.Precision.HIGHEST)
    spread = jnp.einsum("ia,ajk->ijk", pick_x, along_y, precision=lax.Precision.HIGHEST)
    return spread > 0.5


def global_max(value):
    for axis in ("gy", "gx", "gz"):
        value = lax.pmax(value, axis)
    return value


def local(hydro_state, material_id, block_mask):
    extent_x, extent_y, extent_z = material_id.shape
    active = local_active(block_mask, extent_x, extent_y, extent_z)

    def cycle(cycle_number, state_now):
        pressure, sound_speed = equation_of_state(state_now[0], state_now[4], material_id)
        velocity = state_now[1:4]
        vel_faces = [faces(velocity, column) for column in range(3)]
        local_fast = jnp.max(
            sound_speed + jnp.abs(state_now[1]) + jnp.abs(state_now[2]) + jnp.abs(state_now[3])
        )
        fastest = global_max(local_fast)
        step_dt = courant / fastest
        stress, diverge, power, heating = stress_terms(
            velocity, vel_faces, state_now[0], pressure, sound_speed
        )
        accel = acceleration(stress, state_now[0])
        conserved = lagrange(state_now, state_now[0], accel, diverge, power, heating, step_dt)
        remapped = remap(conserved, velocity, vel_faces, step_dt)
        return jnp.where(active[None], remapped, state_now)

    return lax.fori_loop(0, CYCLES, cycle, hydro_state)


def solution(mesh):
    in_specs = (P(None, "gx", "gy", "gz"), P("gx", "gy", "gz"), P())
    out_specs = P(None, "gx", "gy", "gz")
    return jax.shard_map(local, mesh=mesh, in_specs=in_specs, out_specs=out_specs, check_vma=False)
```

```python
import jax
import jax.numpy as jnp
from jax import lax
from jax.sharding import PartitionSpec as P

B = 32
CYCLES = 2


courant = 0.15
visc_quad = 2.0
visc_linear = 0.5
rest_density = (1.0, 1.25, 1.5, 1.8)
sound_base = (1.0, 0.8, 1.2, 0.9)
hugoniot_slope = (1.5, 1.4, 1.2, 1.6)
gruneisen = (2.0, 1.7, 1.6, 2.2)

Z_AXES = ("gz_hi", "gz_lo")
SPATIAL = (("gx", 1), ("gy", 2), (Z_AXES, 3))
STRESS_ROWS = ((0, 3, 4), (3, 1, 5), (4, 5, 2))


def faces(array, j):
    axis, dim = SPATIAL[j]
    peers, length = lax.axis_size(axis), array.shape[dim]
    up = [(i, i + 1) for i in range(peers - 1)]
    down = [(i + 1, i) for i in range(peers - 1)]
    first = lax.slice_in_dim(array, 0, 1, axis=dim)
    last = lax.slice_in_dim(array, length - 1, length, axis=dim)
    from_prev = lax.ppermute(last, axis, up)
    from_next = lax.ppermute(first, axis, down)
    return from_next, from_prev


def plus(array, j, from_next):
    dim = SPATIAL[j][1] - (4 - array.ndim)
    length = array.shape[dim]
    return jnp.concatenate([lax.slice_in_dim(array, 1, length, axis=dim), from_next], axis=dim)


def minus(array, j, from_prev):
    dim = SPATIAL[j][1] - (4 - array.ndim)
    length = array.shape[dim]
    return jnp.concatenate([from_prev, lax.slice_in_dim(array, 0, length - 1, axis=dim)], axis=dim)


def lookup(material, values):
    result = jnp.zeros(material.shape, jnp.float32)
    for number, amount in enumerate(values):
        result = result + jnp.where(material == number, jnp.float32(amount), jnp.float32(0.0))
    return result


def equation_of_state(density, energy, material):
    rest_rho = lookup(material, rest_density)
    sound_zero = lookup(material, sound_base)
    slope_mat = lookup(material, hugoniot_slope)
    gamma_mat = lookup(material, gruneisen)
    strain = 1.0 - rest_rho / density
    squeeze = jnp.maximum(strain, 0.0)
    hugoniot = (
        rest_rho
        * sound_zero
        * sound_zero
        * strain
        * (1.0 + 2.0 * slope_mat * squeeze + 3.0 * slope_mat * slope_mat * squeeze * squeeze)
    )
    pressure = hugoniot * (1.0 - 0.5 * gamma_mat * strain) + gamma_mat * density * energy
    sound_speed = sound_zero * (1.0 + slope_mat * squeeze)
    return (pressure, sound_speed)


def stress_terms(velocity, vel_faces, density, pressure, sound_speed):
    gradient = [
        (plus(velocity, column, vel_faces[column][0]) - minus(velocity, column, vel_faces[column][1])) * 0.5
        for column in range(3)
    ]
    diverge = gradient[0][0] + gradient[1][1] + gradient[2][2]
    strain_xy = 0.5 * (gradient[1][0] + gradient[0][1])
    strain_xz = 0.5 * (gradient[2][0] + gradient[0][2])
    strain_yz = 0.5 * (gradient[2][1] + gradient[1][2])
    squares = (
        gradient[0][0] * gradient[0][0]
        + gradient[1][1] * gradient[1][1]
        + gradient[2][2] * gradient[2][2]
    )
    squares = squares + 2.0 * (
        strain_xy * strain_xy + strain_xz * strain_xz + strain_yz * strain_yz
    )
    compress = jnp.maximum(-diverge, 0.0)
    viscosity = density * compress * (visc_quad * compress + visc_linear * sound_speed)
    stress = [
        -pressure + viscosity * gradient[0][0],
        -pressure + viscosity * gradient[1][1],
        -pressure + viscosity * gradient[2][2],
        viscosity * strain_xy,
        viscosity * strain_xz,
        viscosity * strain_yz,
    ]
    power = -pressure * diverge + viscosity * squares
    heating = viscosity * squares
    return (stress, diverge, power, heating)


def acceleration(stress, density):
    stress_faces = []
    for column in range(3):
        picked = jnp.stack([stress[c] for c in STRESS_ROWS[column]])
        stress_faces.append((picked, faces(picked, column)))
    results = []
    for row in range(3):
        total = jnp.zeros(density.shape, jnp.float32)
        for column in range(3):
            picked, (from_next, from_prev) = stress_faces[column]
            slot = STRESS_ROWS[column].index(STRESS_ROWS[row][column])
            comp = stress[STRESS_ROWS[row][column]]
            total = total + plus(comp, column, from_next[slot]) - minus(comp, column, from_prev[slot])
        results.append(0.5 * total / density)
    return jnp.stack(results)


def lagrange(state_part, density, accel, diverge, power, heating, step_dt):
    new_density = density / (1.0 + step_dt * diverge)
    velocity = state_part[1:4] + step_dt * accel
    energy = state_part[4] + step_dt * power / density
    plastic = state_part[6] + step_dt * heating / density
    return jnp.concatenate(
        [
            new_density[None],
            new_density[None] * velocity,
            (new_density * energy)[None],
            (new_density * state_part[5])[None],
            (new_density * plastic)[None],
            (new_density * state_part[7])[None],
        ]
    )


def remap(conserved, velocity, vel_faces, step_dt):
    centre = conserved
    total = centre
    for column in range(3):
        cons_next, cons_prev = faces(conserved, column)
        middle_vel = velocity[column]
        ahead_vel = plus(velocity[column], column, vel_faces[column][0][column])
        behind_vel = minus(velocity[column], column, vel_faces[column][1][column])
        upper = step_dt * 0.5 * (middle_vel + ahead_vel)
        lower = step_dt * 0.5 * (behind_vel + middle_vel)
        flux_up = jnp.maximum(upper, 0.0) * centre + jnp.minimum(upper, 0.0) * plus(
            conserved, column, cons_next
        )
        flux_down = (
            jnp.maximum(lower, 0.0) * minus(conserved, column, cons_prev)
            + jnp.minimum(lower, 0.0) * centre
        )
        total = total - (flux_up - flux_down)
    density = total[0]
    return jnp.concatenate([density[None], total[1:] / density])


def block_picks(position, extent, count):
    cells = position * extent + jnp.arange(extent, dtype=jnp.int32)
    return (cells[:, None] // B == jnp.arange(count, dtype=jnp.int32)[None, :]).astype(jnp.float32)


def local_active(block_mask, extent_x, extent_y, extent_z):
    count_x, count_y, count_z = block_mask.shape
    pick_x = block_picks(lax.axis_index("gx"), extent_x, count_x)
    pick_y = block_picks(lax.axis_index("gy"), extent_y, count_y)
    pick_z = block_picks(lax.axis_index(Z_AXES), extent_z, count_z)
    present = (block_mask > 0).astype(jnp.float32)
    along_z = jnp.dot(
        present.reshape(count_x * count_y, count_z), pick_z.T, precision=lax.Precision.HIGHEST
    ).reshape(count_x, count_y, extent_z)
    along_y = jnp.einsum("jb,abk->ajk", pick_y, along_z, precision=lax.Precision.HIGHEST)
    spread = jnp.einsum("ia,ajk->ijk", pick_x, along_y, precision=lax.Precision.HIGHEST)
    return spread > 0.5


def global_max(value):
    for axis in ("gy", "gx", "gz_lo", "gz_hi"):
        value = lax.pmax(value, axis)
    return value


def local(hydro_state, material_id, block_mask):
    extent_x, extent_y, extent_z = material_id.shape
    active = local_active(block_mask, extent_x, extent_y, extent_z)
    state_now = hydro_state
    for cycle_number in range(CYCLES):
        pressure, sound_speed = equation_of_state(state_now[0], state_now[4], material_id)
        velocity = state_now[1:4]
        vel_faces = [faces(velocity, column) for column in range(3)]
        local_fast = jnp.max(
            sound_speed + jnp.abs(state_now[1]) + jnp.abs(state_now[2]) + jnp.abs(state_now[3])
        )
        fastest = global_max(local_fast)
        step_dt = courant / fastest
        stress, diverge, power, heating = stress_terms(
            velocity, vel_faces, state_now[0], pressure, sound_speed
        )
        accel = acceleration(stress, state_now[0])
        conserved = lagrange(state_now, state_now[0], accel, diverge, power, heating, step_dt)
        remapped = remap(conserved, velocity, vel_faces, step_dt)
        state_now = jnp.where(active[None], remapped, state_now)
    return state_now


def solution(mesh):
    size_z = mesh.shape["gz"]
    lo = 4 if size_z % 4 == 0 else 1
    split = jax.sharding.Mesh(
        mesh.devices.reshape(size_z // lo, lo, mesh.shape["gx"], mesh.shape["gy"]),
        ("gz_hi", "gz_lo", "gx", "gy"),
    )
    in_specs = (P(None, "gx", "gy", Z_AXES), P("gx", "gy", Z_AXES), P())
    out_specs = P(None, "gx", "gy", Z_AXES)
    return jax.shard_map(local, mesh=split, in_specs=in_specs, out_specs=out_specs, check_vma=False)
```

```python
import jax
import jax.numpy as jnp
from jax import lax
from jax.sharding import PartitionSpec as P

B = 32
CYCLES = 2


courant = 0.15
visc_quad = 2.0
visc_linear = 0.5
rest_density = (1.0, 1.25, 1.5, 1.8)
sound_base = (1.0, 0.8, 1.2, 0.9)
hugoniot_slope = (1.5, 1.4, 1.2, 1.6)
gruneisen = (2.0, 1.7, 1.6, 2.2)

Z_AXES = ("gz_hi", "gz_lo")
SPATIAL = (("gx", 1), ("gy", 2), (Z_AXES, 3))
STRESS_ROWS = ((0, 3, 4), (3, 1, 5), (4, 5, 2))


def faces(array, j):
    axis, dim = SPATIAL[j]
    peers, length = lax.axis_size(axis), array.shape[dim]
    up = [(i, i + 1) for i in range(peers - 1)]
    down = [(i + 1, i) for i in range(peers - 1)]
    first = lax.slice_in_dim(array, 0, 1, axis=dim)
    last = lax.slice_in_dim(array, length - 1, length, axis=dim)
    from_prev = lax.ppermute(last, axis, up)
    from_next = lax.ppermute(first, axis, down)
    return from_next, from_prev


def plus(array, j, from_next):
    dim = SPATIAL[j][1] - (4 - array.ndim)
    length = array.shape[dim]
    return jnp.concatenate([lax.slice_in_dim(array, 1, length, axis=dim), from_next], axis=dim)


def minus(array, j, from_prev):
    dim = SPATIAL[j][1] - (4 - array.ndim)
    length = array.shape[dim]
    return jnp.concatenate([from_prev, lax.slice_in_dim(array, 0, length - 1, axis=dim)], axis=dim)


def lookup(material, values):
    result = jnp.zeros(material.shape, jnp.float32)
    for number, amount in enumerate(values):
        result = result + jnp.where(material == number, jnp.float32(amount), jnp.float32(0.0))
    return result


def equation_of_state(density, energy, material):
    rest_rho = lookup(material, rest_density)
    sound_zero = lookup(material, sound_base)
    slope_mat = lookup(material, hugoniot_slope)
    gamma_mat = lookup(material, gruneisen)
    strain = 1.0 - rest_rho / density
    squeeze = jnp.maximum(strain, 0.0)
    hugoniot = (
        rest_rho
        * sound_zero
        * sound_zero
        * strain
        * (1.0 + 2.0 * slope_mat * squeeze + 3.0 * slope_mat * slope_mat * squeeze * squeeze)
    )
    pressure = hugoniot * (1.0 - 0.5 * gamma_mat * strain) + gamma_mat * density * energy
    sound_speed = sound_zero * (1.0 + slope_mat * squeeze)
    return (pressure, sound_speed)


def stress_terms(velocity, vel_faces, density, pressure, sound_speed):
    gradient = [
        (plus(velocity, column, vel_faces[column][0]) - minus(velocity, column, vel_faces[column][1])) * 0.5
        for column in range(3)
    ]
    diverge = gradient[0][0] + gradient[1][1] + gradient[2][2]
    strain_xy = 0.5 * (gradient[1][0] + gradient[0][1])
    strain_xz = 0.5 * (gradient[2][0] + gradient[0][2])
    strain_yz = 0.5 * (gradient[2][1] + gradient[1][2])
    squares = (
        gradient[0][0] * gradient[0][0]
        + gradient[1][1] * gradient[1][1]
        + gradient[2][2] * gradient[2][2]
    )
    squares = squares + 2.0 * (
        strain_xy * strain_xy + strain_xz * strain_xz + strain_yz * strain_yz
    )
    compress = jnp.maximum(-diverge, 0.0)
    viscosity = density * compress * (visc_quad * compress + visc_linear * sound_speed)
    stress = [
        -pressure + viscosity * gradient[0][0],
        -pressure + viscosity * gradient[1][1],
        -pressure + viscosity * gradient[2][2],
        viscosity * strain_xy,
        viscosity * strain_xz,
        viscosity * strain_yz,
    ]
    power = -pressure * diverge + viscosity * squares
    heating = viscosity * squares
    return (stress, diverge, power, heating)


def acceleration(stress, density):
    stress_faces = []
    for column in range(3):
        picked = jnp.stack([stress[c] for c in STRESS_ROWS[column]])
        stress_faces.append((picked, faces(picked, column)))
    results = []
    for row in range(3):
        total = jnp.zeros(density.shape, jnp.float32)
        for column in range(3):
            picked, (from_next, from_prev) = stress_faces[column]
            slot = STRESS_ROWS[column].index(STRESS_ROWS[row][column])
            comp = stress[STRESS_ROWS[row][column]]
            total = total + plus(comp, column, from_next[slot]) - minus(comp, column, from_prev[slot])
        results.append(0.5 * total / density)
    return jnp.stack(results)


def lagrange(state_part, density, accel, diverge, power, heating, step_dt):
    new_density = density / (1.0 + step_dt * diverge)
    velocity = state_part[1:4] + step_dt * accel
    energy = state_part[4] + step_dt * power / density
    plastic = state_part[6] + step_dt * heating / density
    return jnp.concatenate(
        [
            new_density[None],
            new_density[None] * velocity,
            (new_density * energy)[None],
            (new_density * state_part[5])[None],
            (new_density * plastic)[None],
            (new_density * state_part[7])[None],
        ]
    )


def remap(conserved, velocity, vel_faces, step_dt):
    centre = conserved
    total = centre
    for column in range(3):
        cons_next, cons_prev = faces(conserved, column)
        middle_vel = velocity[column]
        ahead_vel = plus(velocity[column], column, vel_faces[column][0][column])
        behind_vel = minus(velocity[column], column, vel_faces[column][1][column])
        upper = step_dt * 0.5 * (middle_vel + ahead_vel)
        lower = step_dt * 0.5 * (behind_vel + middle_vel)
        flux_up = jnp.maximum(upper, 0.0) * centre + jnp.minimum(upper, 0.0) * plus(
            conserved, column, cons_next
        )
        flux_down = (
            jnp.maximum(lower, 0.0) * minus(conserved, column, cons_prev)
            + jnp.minimum(lower, 0.0) * centre
        )
        total = total - (flux_up - flux_down)
    density = total[0]
    return jnp.concatenate([density[None], total[1:] / density])


def block_picks(position, extent, count):
    cells = position * extent + jnp.arange(extent, dtype=jnp.int32)
    return (cells[:, None] // B == jnp.arange(count, dtype=jnp.int32)[None, :]).astype(jnp.float32)


def local_active(block_mask, extent_x, extent_y, extent_z):
    count_x, count_y, count_z = block_mask.shape
    pick_x = block_picks(lax.axis_index("gx"), extent_x, count_x)
    pick_y = block_picks(lax.axis_index("gy"), extent_y, count_y)
    pick_z = block_picks(lax.axis_index(Z_AXES), extent_z, count_z)
    present = (block_mask > 0).astype(jnp.float32)
    along_z = jnp.dot(
        present.reshape(count_x * count_y, count_z), pick_z.T, precision=lax.Precision.HIGHEST
    ).reshape(count_x, count_y, extent_z)
    along_y = jnp.einsum("jb,abk->ajk", pick_y, along_z, precision=lax.Precision.HIGHEST)
    spread = jnp.einsum("ia,ajk->ijk", pick_x, along_y, precision=lax.Precision.HIGHEST)
    return spread > 0.5


def global_max(value):
    wide = jnp.broadcast_to(value, (65536,))
    return lax.pmax(wide, ("gz_hi", "gz_lo", "gx", "gy"))[0]


def local(hydro_state, material_id, block_mask):
    extent_x, extent_y, extent_z = material_id.shape
    active = local_active(block_mask, extent_x, extent_y, extent_z)
    state_now = hydro_state
    for cycle_number in range(CYCLES):
        pressure, sound_speed = equation_of_state(state_now[0], state_now[4], material_id)
        velocity = state_now[1:4]
        vel_faces = [faces(velocity, column) for column in range(3)]
        local_fast = jnp.max(
            sound_speed + jnp.abs(state_now[1]) + jnp.abs(state_now[2]) + jnp.abs(state_now[3])
        )
        fastest = global_max(local_fast)
        step_dt = courant / fastest
        stress, diverge, power, heating = stress_terms(
            velocity, vel_faces, state_now[0], pressure, sound_speed
        )
        accel = acceleration(stress, state_now[0])
        conserved = lagrange(state_now, state_now[0], accel, diverge, power, heating, step_dt)
        remapped = remap(conserved, velocity, vel_faces, step_dt)
        state_now = jnp.where(active[None], remapped, state_now)
    return state_now


def solution(mesh):
    size_z = mesh.shape["gz"]
    lo = 4 if size_z % 4 == 0 else 1
    split = jax.sharding.Mesh(
        mesh.devices.reshape(size_z // lo, lo, mesh.shape["gx"], mesh.shape["gy"]),
        ("gz_hi", "gz_lo", "gx", "gy"),
    )
    in_specs = (P(None, "gx", "gy", Z_AXES), P("gx", "gy", Z_AXES), P())
    out_specs = P(None, "gx", "gy", Z_AXES)
    return jax.shard_map(local, mesh=split, in_specs=in_specs, out_specs=out_specs, check_vma=False)
```

```python
import jax
import jax.numpy as jnp
from jax import lax
from jax.sharding import PartitionSpec as P

B = 32
CYCLES = 2


courant = 0.15
visc_quad = 2.0
visc_linear = 0.5
rest_density = (1.0, 1.25, 1.5, 1.8)
sound_base = (1.0, 0.8, 1.2, 0.9)
hugoniot_slope = (1.5, 1.4, 1.2, 1.6)
gruneisen = (2.0, 1.7, 1.6, 2.2)

Z_AXES = ("gz_hi", "gz_lo")
X_AXES = ("gx_hi", "gx_lo")
SPATIAL = ((X_AXES, 1), ("gy", 2), (Z_AXES, 3))
STRESS_ROWS = ((0, 3, 4), (3, 1, 5), (4, 5, 2))


def faces(array, j):
    axis, dim = SPATIAL[j]
    peers, length = lax.axis_size(axis), array.shape[dim]
    up = [(i, i + 1) for i in range(peers - 1)]
    down = [(i + 1, i) for i in range(peers - 1)]
    first = lax.slice_in_dim(array, 0, 1, axis=dim)
    last = lax.slice_in_dim(array, length - 1, length, axis=dim)
    from_prev = lax.ppermute(last, axis, up)
    from_next = lax.ppermute(first, axis, down)
    return from_next, from_prev


def plus(array, j, from_next):
    dim = SPATIAL[j][1] - (4 - array.ndim)
    length = array.shape[dim]
    return jnp.concatenate([lax.slice_in_dim(array, 1, length, axis=dim), from_next], axis=dim)


def minus(array, j, from_prev):
    dim = SPATIAL[j][1] - (4 - array.ndim)
    length = array.shape[dim]
    return jnp.concatenate([from_prev, lax.slice_in_dim(array, 0, length - 1, axis=dim)], axis=dim)


def lookup(material, values):
    result = jnp.zeros(material.shape, jnp.float32)
    for number, amount in enumerate(values):
        result = result + jnp.where(material == number, jnp.float32(amount), jnp.float32(0.0))
    return result


def equation_of_state(density, energy, material):
    rest_rho = lookup(material, rest_density)
    sound_zero = lookup(material, sound_base)
    slope_mat = lookup(material, hugoniot_slope)
    gamma_mat = lookup(material, gruneisen)
    strain = 1.0 - rest_rho / density
    squeeze = jnp.maximum(strain, 0.0)
    hugoniot = (
        rest_rho
        * sound_zero
        * sound_zero
        * strain
        * (1.0 + 2.0 * slope_mat * squeeze + 3.0 * slope_mat * slope_mat * squeeze * squeeze)
    )
    pressure = hugoniot * (1.0 - 0.5 * gamma_mat * strain) + gamma_mat * density * energy
    sound_speed = sound_zero * (1.0 + slope_mat * squeeze)
    return (pressure, sound_speed)


def stress_terms(velocity, vel_faces, density, pressure, sound_speed):
    gradient = [
        (plus(velocity, column, vel_faces[column][0]) - minus(velocity, column, vel_faces[column][1])) * 0.5
        for column in range(3)
    ]
    diverge = gradient[0][0] + gradient[1][1] + gradient[2][2]
    strain_xy = 0.5 * (gradient[1][0] + gradient[0][1])
    strain_xz = 0.5 * (gradient[2][0] + gradient[0][2])
    strain_yz = 0.5 * (gradient[2][1] + gradient[1][2])
    squares = (
        gradient[0][0] * gradient[0][0]
        + gradient[1][1] * gradient[1][1]
        + gradient[2][2] * gradient[2][2]
    )
    squares = squares + 2.0 * (
        strain_xy * strain_xy + strain_xz * strain_xz + strain_yz * strain_yz
    )
    compress = jnp.maximum(-diverge, 0.0)
    viscosity = density * compress * (visc_quad * compress + visc_linear * sound_speed)
    stress = [
        -pressure + viscosity * gradient[0][0],
        -pressure + viscosity * gradient[1][1],
        -pressure + viscosity * gradient[2][2],
        viscosity * strain_xy,
        viscosity * strain_xz,
        viscosity * strain_yz,
    ]
    power = -pressure * diverge + viscosity * squares
    heating = viscosity * squares
    return (stress, diverge, power, heating)


def acceleration(stress, density):
    stress_faces = []
    for column in range(3):
        picked = jnp.stack([stress[c] for c in STRESS_ROWS[column]])
        stress_faces.append((picked, faces(picked, column)))
    results = []
    for row in range(3):
        total = jnp.zeros(density.shape, jnp.float32)
        for column in range(3):
            picked, (from_next, from_prev) = stress_faces[column]
            slot = STRESS_ROWS[column].index(STRESS_ROWS[row][column])
            comp = stress[STRESS_ROWS[row][column]]
            total = total + plus(comp, column, from_next[slot]) - minus(comp, column, from_prev[slot])
        results.append(0.5 * total / density)
    return jnp.stack(results)


def lagrange(state_part, density, accel, diverge, power, heating, step_dt):
    new_density = density / (1.0 + step_dt * diverge)
    velocity = state_part[1:4] + step_dt * accel
    energy = state_part[4] + step_dt * power / density
    plastic = state_part[6] + step_dt * heating / density
    return jnp.concatenate(
        [
            new_density[None],
            new_density[None] * velocity,
            (new_density * energy)[None],
            (new_density * state_part[5])[None],
            (new_density * plastic)[None],
            (new_density * state_part[7])[None],
        ]
    )


def remap(conserved, velocity, vel_faces, step_dt):
    centre = conserved
    total = centre
    for column in range(3):
        cons_next, cons_prev = faces(conserved, column)
        middle_vel = velocity[column]
        ahead_vel = plus(velocity[column], column, vel_faces[column][0][column])
        behind_vel = minus(velocity[column], column, vel_faces[column][1][column])
        upper = step_dt * 0.5 * (middle_vel + ahead_vel)
        lower = step_dt * 0.5 * (behind_vel + middle_vel)
        flux_up = jnp.maximum(upper, 0.0) * centre + jnp.minimum(upper, 0.0) * plus(
            conserved, column, cons_next
        )
        flux_down = (
            jnp.maximum(lower, 0.0) * minus(conserved, column, cons_prev)
            + jnp.minimum(lower, 0.0) * centre
        )
        total = total - (flux_up - flux_down)
    density = total[0]
    return jnp.concatenate([density[None], total[1:] / density])


def block_picks(position, extent, count):
    cells = position * extent + jnp.arange(extent, dtype=jnp.int32)
    return (cells[:, None] // B == jnp.arange(count, dtype=jnp.int32)[None, :]).astype(jnp.float32)


def local_active(block_mask, extent_x, extent_y, extent_z):
    count_x, count_y, count_z = block_mask.shape
    pick_x = block_picks(lax.axis_index(X_AXES), extent_x, count_x)
    pick_y = block_picks(lax.axis_index("gy"), extent_y, count_y)
    pick_z = block_picks(lax.axis_index(Z_AXES), extent_z, count_z)
    present = (block_mask > 0).astype(jnp.float32)
    along_z = jnp.dot(
        present.reshape(count_x * count_y, count_z), pick_z.T, precision=lax.Precision.HIGHEST
    ).reshape(count_x, count_y, extent_z)
    along_y = jnp.einsum("jb,abk->ajk", pick_y, along_z, precision=lax.Precision.HIGHEST)
    spread = jnp.einsum("ia,ajk->ijk", pick_x, along_y, precision=lax.Precision.HIGHEST)
    return spread > 0.5


def global_max(value):
    for axis in ("gy", "gx_lo", "gx_hi", "gz_lo", "gz_hi"):
        value = lax.pmax(value, axis)
    return value


def local(hydro_state, material_id, block_mask):
    extent_x, extent_y, extent_z = material_id.shape
    active = local_active(block_mask, extent_x, extent_y, extent_z)
    state_now = hydro_state
    for cycle_number in range(CYCLES):
        pressure, sound_speed = equation_of_state(state_now[0], state_now[4], material_id)
        velocity = state_now[1:4]
        vel_faces = [faces(velocity, column) for column in range(3)]
        local_fast = jnp.max(
            sound_speed + jnp.abs(state_now[1]) + jnp.abs(state_now[2]) + jnp.abs(state_now[3])
        )
        fastest = global_max(local_fast)
        step_dt = courant / fastest
        stress, diverge, power, heating = stress_terms(
            velocity, vel_faces, state_now[0], pressure, sound_speed
        )
        accel = acceleration(stress, state_now[0])
        conserved = lagrange(state_now, state_now[0], accel, diverge, power, heating, step_dt)
        remapped = remap(conserved, velocity, vel_faces, step_dt)
        state_now = jnp.where(active[None], remapped, state_now)
    return state_now


def solution(mesh):
    size_z, size_x = mesh.shape["gz"], mesh.shape["gx"]
    lo = 4 if size_z % 4 == 0 else 1
    pair = 2 if size_x % 2 == 0 else 1
    split = jax.sharding.Mesh(
        mesh.devices.reshape(size_z // lo, lo, size_x // pair, pair, mesh.shape["gy"]),
        ("gz_hi", "gz_lo", "gx_hi", "gx_lo", "gy"),
    )
    in_specs = (P(None, X_AXES, "gy", Z_AXES), P(X_AXES, "gy", Z_AXES), P())
    out_specs = P(None, X_AXES, "gy", Z_AXES)
    return jax.shard_map(local, mesh=split, in_specs=in_specs, out_specs=out_specs, check_vma=False)
```
